32 devices in a mesh: groups: 2 (over y), col: 8 (over z, x), row: 2 (over core).
Axes of the slice: x: 2, y: 2, z: 4, core: 2. Of those that a mesh axis runs over, the one named last changes fastest.
Arguments:
- down_proj: float32 [8, 2048, 7168], P(('groups', 'row'), 'col'), parts along dimension 0, may hold values from -8 to 8
- act_scale: float32 [8, 2048], P(('groups', 'row'), 'col'), parts along dimension 0, may hold values from 0.5 to 4
- block_order: int32 [512], P('groups'), parts along dimension 0, may hold values from 0 to 255, each once
Outputs:
- rotated: float32 [512, 28, 4, 2048], P(('groups', 'col'), None, 'row'), parts along dimension 0
The draws below stay inside these ranges and needn't reach their ends.
There are 2 independent parts, one for each index of `groups`. The reference program is written for one: setup_inputs(seed, part) draws one part's arguments, and reference() takes and returns one part's arrays. A program takes and returns all parts, laid end to end along the dimension named above; each array names one. Nothing has to cross between parts.
Inputs may be any that keep to these rules, and one draw needn't show every extreme that they name: `block_order`: every block number appears exactly once.
All inputs are finite; a program needn't handle non-finite values.
Results may differ from the reference program's by a relative error of at most 0.000078.
Values sent between devices are 32-bit elements; how exact they have to be, the bound alone decides.
No kernel may reach another device: no remote copies, remote signals or barrier semaphores. Data moves between devices by JAX's collectives and lax.ppermute only.
A program may use at most 128 MiB of HBM per device.

```python
import math
import jax
import jax.numpy as jnp
from jax import lax

D = 7168
FF = 2048
BLK = 28
EXPERTS = 4
NB = 256


def draw_down_proj(key, part):
    key_noise, key_column, key_rowpart, key_colpart = jax.random.split(jax.random.fold_in(key, 17), 4)
    shape = (EXPERTS, FF, D)
    noise = jnp.clip(jax.random.normal(key_noise, shape, jnp.float32), -4.0, 4.0)
    common_weight = 0.4
    column = jnp.exp(jax.random.uniform(key_column, (D,), jnp.float32, 0.0, 0.9))
    row_common = jnp.clip(jax.random.normal(key_rowpart, (EXPERTS, FF, 1), jnp.float32), -4.0, 4.0)
    col_common = jnp.clip(jax.random.normal(key_colpart, (D,), jnp.float32), -4.0, 4.0)
    values = 0.4 * (noise * column + common_weight * row_common * col_common)
    return values.astype(jnp.float32)


def block_levels(stream_key, shape, cuts, low, high):
    loudness = 1.0
    for position, shards_of in cuts:
        heights = jax.random.uniform(jax.random.fold_in(jax.random.fold_in(stream_key, 6), position), (shards_of,), jnp.float32, low / len(cuts), high / len(cuts))
        loudness = loudness * jnp.repeat(jnp.exp(heights), shape[position] // shards_of).reshape((-1,) + (1,) * (len(shape) - 1 - position))
    return loudness


def setup_inputs(seed: int = 0, part: int = 0) -> dict:
    key_list = jax.random.split(jax.random.key(seed), 4)
    part_splits = jax.random.split(jax.random.fold_in(key_list[3], part), 4)
    down_proj = draw_down_proj(jax.random.fold_in(jax.random.fold_in(key_list[3], part), 71), part)
    act_scale = jnp.clip(jnp.exp(math.log(4.0) - 2.0794415 * jax.random.uniform(part_splits[1], (EXPERTS, FF), jnp.float32) ** block_levels(part_splits[1], (EXPERTS, FF), ((0, 2), (1, 8)), -0.2, 0.2)), 0.5, 4.0)
    block_order = jax.random.permutation(part_splits[2], NB).astype(jnp.int32)
    return {"down_proj": down_proj, "act_scale": act_scale, "block_order": block_order}


highest = lax.Precision.HIGHEST

def joint_rotation(gram_matrix):
    square = jnp.einsum('pij,pjk->pik', gram_matrix, gram_matrix, precision=highest)
    lower_factor = jnp.linalg.cholesky(square)
    solved = lax.linalg.triangular_solve(lower_factor, gram_matrix, left_side=True, lower=True)
    return jnp.swapaxes(solved, 1, 2)

def jacobi_step(panels):
    gram_matrix = jnp.einsum('pkr,plr->pkl', panels, panels, precision=highest)
    rotation = joint_rotation(gram_matrix)
    return jnp.einsum('pkl,pkr->plr', rotation, panels, precision=highest)

def reference(down_proj, act_scale, block_order):
    block_count = D // BLK
    scaled = down_proj * act_scale[:, :, None]
    blocks = scaled.reshape(EXPERTS * FF, block_count, BLK)
    ordered = jnp.take(blocks, block_order.astype(jnp.int32), axis=1)
    panels = jnp.transpose(ordered, (1, 2, 0)).reshape(block_count // 2, 2 * BLK, EXPERTS * FF)
    first_pass = jacobi_step(panels)
    leading = first_pass[:, :BLK]
    trailing = first_pass[:, BLK:]
    moved = jnp.roll(leading, 1, axis=0)
    second_pass = jacobi_step(jnp.concatenate([moved, trailing], axis=1))
    return second_pass.reshape(block_count, BLK, EXPERTS, FF)
```

```python
import jax
import jax.numpy as jnp
from jax import lax
from jax.experimental import pallas as pl
from jax.experimental.pallas import tpu as pltpu
from jax.sharding import PartitionSpec as P

BLK = 28


highest = lax.Precision.HIGHEST


def from_behind(block, axis, distance):
    devices = range(lax.axis_size(axis))
    route = [((i - distance) % len(devices), i) for i in devices]
    return lax.ppermute(block, axis, route)


def chol_solve_kernel(sq_ref, s_ref, x_ref, a_ref):
    n = sq_ref.shape[1]
    a_ref[...] = sq_ref[...]
    x_ref[...] = s_ref[...]
    for k in range(n):
        r0 = (k // 8) * 8
        rows = n - r0
        i_idx = lax.broadcasted_iota(jnp.int32, (1, rows, 1), 1) + r0
        j_idx = lax.broadcasted_iota(jnp.int32, (1, 1, n), 2)
        a_part = a_ref[:, r0:, :]
        d = jnp.sqrt(a_ref[:, k:k + 1, k:k + 1])
        lcol = jnp.where(i_idx >= k, a_part[:, :, k:k + 1] / d, 0.0)
        lrow = jnp.where(j_idx >= k, a_ref[:, k:k + 1, :] / d, 0.0)
        a_ref[:, r0:, :] = a_part - lcol * lrow
        xk = x_ref[:, k:k + 1, :] / d
        b_part = x_ref[:, r0:, :]
        b_part = b_part - jnp.where(i_idx > k, lcol, 0.0) * xk
        x_ref[:, r0:, :] = jnp.where(i_idx == k, xk, b_part)


def chol_solve(square, gram_matrix):
    batch, n, _ = gram_matrix.shape
    spec = pl.BlockSpec((batch, n, n), lambda: (0, 0, 0))
    return pl.pallas_call(
        chol_solve_kernel,
        out_shape=jax.ShapeDtypeStruct(gram_matrix.shape, jnp.float32),
        in_specs=[spec, spec],
        out_specs=spec,
        scratch_shapes=[pltpu.VMEM((batch, n, n), jnp.float32)],
    )(square, gram_matrix)


def solved_rotation(gram_matrix):
    square = jnp.einsum("pij,pjk->pik", gram_matrix, gram_matrix, precision=highest)
    return chol_solve(square, gram_matrix)


def pair_gram(panels):
    return jnp.einsum("pkr,plr->pkl", panels, panels, precision=highest)


def rotate_pairs(solved, panels):
    return jnp.einsum("plk,pkr->plr", solved, panels, precision=highest)


def local_panels(piece):
    panels = piece.reshape(piece.shape[1], piece.shape[2], -1)
    return (panels, pair_gram(panels))


def outgoing_panels(blocks, picked, col_count, extent):
    experts_here, hidden_here = (blocks.shape[0], blocks.shape[1])
    ordered = jnp.take(blocks, picked, axis=2)
    ordered = ordered.reshape(experts_here, hidden_here, col_count, extent // 2, 2 * BLK)
    ordered = jnp.transpose(ordered, (2, 3, 4, 0, 1))
    return ordered.reshape(col_count, extent // 2, 2 * BLK, experts_here, 1, hidden_here)


def shards(down_proj, act_scale, block_order):
    col_count = lax.axis_size("col")
    experts_here, hidden_here, width = down_proj.shape
    block_count = width // BLK
    per_device = block_count // col_count
    scaled = down_proj * act_scale[:, :, None]
    blocks = scaled.reshape(experts_here, hidden_here, block_count, BLK)
    sending = outgoing_panels(blocks, block_order, col_count, per_device)
    panels, partial_sums = local_panels(
        lax.all_to_all(sending, "col", split_axis=0, concat_axis=4, tiled=True)
    )
    gram_all = lax.psum(partial_sums, "row")
    first_pass = rotate_pairs(solved_rotation(gram_all), panels)
    leading = first_pass[:, :BLK]
    trailing = first_pass[:, BLK:]
    carried = from_behind(leading[-1:], "col", 1)
    moved = jnp.concatenate([carried, leading[:-1]], axis=0)
    next_panels = jnp.concatenate([moved, trailing], axis=1)
    next_total = lax.psum(pair_gram(next_panels), "row")
    second_pass = rotate_pairs(solved_rotation(next_total), next_panels)
    return second_pass.reshape(per_device, BLK, experts_here, -1)


def solution(mesh):
    return jax.shard_map(
        shards,
        mesh=mesh,
        in_specs=(P(("groups", "row"), "col", None), P(("groups", "row"), "col"), P("groups")),
        out_specs=P(("groups", "col"), None, "row", None),
        check_vma=False,
    )
```

```python
import jax
import jax.numpy as jnp
from jax import lax
from jax.experimental import pallas as pl
from jax.experimental.pallas import tpu as pltpu
from jax.sharding import PartitionSpec as P

BLK = 28


highest = lax.Precision.HIGHEST


def chol_solve_kernel(sq_ref, s_ref, x_ref, a_ref):
    n = sq_ref.shape[1]
    a_ref[...] = sq_ref[...]
    x_ref[...] = s_ref[...]
    for k in range(n):
        r0 = (k // 8) * 8
        rows = n - r0
        i_idx = lax.broadcasted_iota(jnp.int32, (1, rows, 1), 1) + r0
        j_idx = lax.broadcasted_iota(jnp.int32, (1, 1, n), 2)
        a_part = a_ref[:, r0:, :]
        d = jnp.sqrt(a_ref[:, k:k + 1, k:k + 1])
        lcol = jnp.where(i_idx >= k, a_part[:, :, k:k + 1] / d, 0.0)
        lrow = jnp.where(j_idx >= k, a_ref[:, k:k + 1, :] / d, 0.0)
        a_ref[:, r0:, :] = a_part - lcol * lrow
        xk = x_ref[:, k:k + 1, :] / d
        b_part = x_ref[:, r0:, :]
        b_part = b_part - jnp.where(i_idx > k, lcol, 0.0) * xk
        x_ref[:, r0:, :] = jnp.where(i_idx == k, xk, b_part)


def chol_solve(square, gram_matrix):
    batch, n, _ = gram_matrix.shape
    spec = pl.BlockSpec((batch, n, n), lambda: (0, 0, 0))
    return pl.pallas_call(
        chol_solve_kernel,
        out_shape=jax.ShapeDtypeStruct(gram_matrix.shape, jnp.float32),
        in_specs=[spec, spec],
        out_specs=spec,
        scratch_shapes=[pltpu.VMEM((batch, n, n), jnp.float32)],
    )(square, gram_matrix)


def mm(spec, a, b):
    return jnp.einsum(spec, a, b, precision=highest)


def solved_rotation(gram_matrix):
    return chol_solve(mm("pij,pjk->pik", gram_matrix, gram_matrix), gram_matrix)


def shards(down_proj, act_scale, block_order):
    col_count = lax.axis_size("col")
    me = lax.axis_index("col")
    experts_here, hidden_here, width = down_proj.shape
    block_count = width // BLK
    per_device = block_count // col_count
    panels_here = per_device // 2
    rows_here = experts_here * hidden_here
    scaled = down_proj * act_scale[:, :, None]
    blocks = scaled.reshape(experts_here, hidden_here, block_count, BLK)
    span = jnp.arange(per_device + 2, dtype=jnp.int32)

    received = []
    for d in range(col_count):
        dest = (me + d) % col_count
        picked = jnp.take(block_order, (dest * per_device - 2 + span) % block_count)
        piece = jnp.take(blocks, picked, axis=2)
        piece = jnp.transpose(piece, (2, 3, 0, 1)).reshape(panels_here + 1, 2 * BLK, rows_here)
        if d:
            route = [(i, (i + d) % col_count) for i in range(col_count)]
            piece = lax.ppermute(piece, "col", route)
        received.append(piece)

    grams = sum(mm("pkr,plr->pkl", r, r) for r in received)
    cross = sum(mm("pkr,plr->pkl", r[:-1], r[1:]) for r in received)
    totals = lax.psum(jnp.concatenate([grams, cross], axis=0), "row")
    grams, cross = totals[: panels_here + 1], totals[panels_here + 1:]

    first = solved_rotation(grams)
    top = first[:-1, :BLK]
    bottom = first[1:, BLK:]
    g_top = mm("pik,pjk->pij", mm("pik,pkl->pil", top, grams[:-1]), top)
    g_bottom = mm("pik,pjk->pij", mm("pik,pkl->pil", bottom, grams[1:]), bottom)
    g_cross = mm("pik,pjk->pij", mm("pik,pkl->pil", top, cross), bottom)
    second_gram = jnp.concatenate(
        [
            jnp.concatenate([g_top, g_cross], axis=2),
            jnp.concatenate([jnp.swapaxes(g_cross, 1, 2), g_bottom], axis=2),
        ],
        axis=1,
    )
    second = solved_rotation(second_gram)
    lead = mm("plk,pkm->plm", second[:, :, :BLK], top)
    trail = mm("plk,pkm->plm", second[:, :, BLK:], bottom)

    out = jnp.zeros((per_device, BLK, experts_here, hidden_here * col_count), jnp.float32)
    for d, r in enumerate(received):
        src = (me - d) % col_count
        part = mm("plk,pkr->plr", lead, r[:-1]) + mm("plk,pkr->plr", trail, r[1:])
        part = part.reshape(per_device, BLK, experts_here, hidden_here)
        out = lax.dynamic_update_slice(out, part, (0, 0, 0, src * hidden_here))
    return out


def solution(mesh):
    return jax.shard_map(
        shards,
        mesh=mesh,
        in_specs=(P(("groups", "row"), "col", None), P(("groups", "row"), "col"), P("groups")),
        out_specs=P(("groups", "col"), None, "row", None),
        check_vma=False,
    )
```

```python
import jax
import jax.numpy as jnp
from jax import lax
from jax.experimental import pallas as pl
from jax.experimental.pallas import tpu as pltpu
from jax.sharding import PartitionSpec as P

BLK = 28


highest = lax.Precision.HIGHEST


def chol_solve_kernel(sq_ref, s_ref, x_ref, a_ref):
    n = sq_ref.shape[1]
    a_ref[...] = sq_ref[...]
    x_ref[...] = s_ref[...]
    for k in range(n):
        r0 = (k // 8) * 8
        rows = n - r0
        i_idx = lax.broadcasted_iota(jnp.int32, (1, rows, 1), 1) + r0
        j_idx = lax.broadcasted_iota(jnp.int32, (1, 1, n), 2)
        a_part = a_ref[:, r0:, :]
        d = jnp.sqrt(a_ref[:, k:k + 1, k:k + 1])
        lcol = jnp.where(i_idx >= k, a_part[:, :, k:k + 1] / d, 0.0)
        lrow = jnp.where(j_idx >= k, a_ref[:, k:k + 1, :] / d, 0.0)
        a_ref[:, r0:, :] = a_part - lcol * lrow
        xk = x_ref[:, k:k + 1, :] / d
        b_part = x_ref[:, r0:, :]
        b_part = b_part - jnp.where(i_idx > k, lcol, 0.0) * xk
        x_ref[:, r0:, :] = jnp.where(i_idx == k, xk, b_part)


def chol_solve(square, gram_matrix):
    batch, n, _ = gram_matrix.shape
    spec = pl.BlockSpec((batch, n, n), lambda: (0, 0, 0))
    return pl.pallas_call(
        chol_solve_kernel,
        out_shape=jax.ShapeDtypeStruct(gram_matrix.shape, jnp.float32),
        in_specs=[spec, spec],
        out_specs=spec,
        scratch_shapes=[pltpu.VMEM((batch, n, n), jnp.float32)],
    )(square, gram_matrix)


def mm(spec, a, b):
    return jnp.einsum(spec, a, b, precision=highest)


def solved_rotation(gram_matrix):
    return chol_solve(mm("pij,pjk->pik", gram_matrix, gram_matrix), gram_matrix)


def sum_over_row(x):
    if lax.axis_size("row") != 2:
        return lax.psum(x, "row")
    return x + lax.ppermute(x, "row", [(0, 1), (1, 0)])


def shards(down_proj, act_scale, block_order):
    col_count = lax.axis_size("col")
    me = lax.axis_index("col")
    experts_here, hidden_here, width = down_proj.shape
    block_count = width // BLK
    per_device = block_count // col_count
    panels_here = per_device // 2
    rows_here = experts_here * hidden_here
    scaled = down_proj * act_scale[:, :, None]
    blocks = scaled.reshape(experts_here, hidden_here, block_count, BLK)
    span = jnp.arange(per_device + 2, dtype=jnp.int32)

    received = []
    for d in range(col_count):
        dest = (me + d) % col_count
        picked = jnp.take(block_order, (dest * per_device - 2 + span) % block_count)
        piece = jnp.take(blocks, picked, axis=2)
        piece = jnp.transpose(piece, (2, 3, 0, 1)).reshape(panels_here + 1, 2 * BLK, rows_here)
        if d:
            route = [(i, (i + d) % col_count) for i in range(col_count)]
            piece = lax.ppermute(piece, "col", route)
        received.append(piece)

    grams = sum(mm("pkr,plr->pkl", r, r) for r in received)
    cross = sum(mm("pkr,plr->pkl", r[:-1], r[1:]) for r in received)
    totals = sum_over_row(jnp.concatenate([grams, cross], axis=0))
    grams, cross = totals[: panels_here + 1], totals[panels_here + 1:]

    first = solved_rotation(grams)
    top = first[:-1, :BLK]
    bottom = first[1:, BLK:]
    g_top = mm("pik,pjk->pij", mm("pik,pkl->pil", top, grams[:-1]), top)
    g_bottom = mm("pik,pjk->pij", mm("pik,pkl->pil", bottom, grams[1:]), bottom)
    g_cross = mm("pik,pjk->pij", mm("pik,pkl->pil", top, cross), bottom)
    second_gram = jnp.concatenate(
        [
            jnp.concatenate([g_top, g_cross], axis=2),
            jnp.concatenate([jnp.swapaxes(g_cross, 1, 2), g_bottom], axis=2),
        ],
        axis=1,
    )
    second = solved_rotation(second_gram)
    lead = mm("plk,pkm->plm", second[:, :, :BLK], top)
    trail = mm("plk,pkm->plm", second[:, :, BLK:], bottom)

    out = jnp.zeros((per_device, BLK, experts_here, hidden_here * col_count), jnp.float32)
    for d, r in enumerate(received):
        src = (me - d) % col_count
        part = mm("plk,pkr->plr", lead, r[:-1]) + mm("plk,pkr->plr", trail, r[1:])
        part = part.reshape(per_device, BLK, experts_here, hidden_here)
        out = lax.dynamic_update_slice(out, part, (0, 0, 0, src * hidden_here))
    return out


def solution(mesh):
    return jax.shard_map(
        shards,
        mesh=mesh,
        in_specs=(P(("groups", "row"), "col", None), P(("groups", "row"), "col"), P("groups")),
        out_specs=P(("groups", "col"), None, "row", None),
        check_vma=False,
    )
```

```python
import jax
import jax.numpy as jnp
from jax import lax
from jax.experimental import pallas as pl
from jax.experimental.pallas import tpu as pltpu
from jax.sharding import PartitionSpec as P

BLK = 28


highest = lax.Precision.HIGHEST


def chol_solve_kernel(sq_ref, s_ref, x_ref, a_ref):
    n = sq_ref.shape[1]
    a_ref[...] = sq_ref[...]
    x_ref[...] = s_ref[...]
    for k in range(n):
        r0 = (k // 8) * 8
        rows = n - r0
        i_idx = lax.broadcasted_iota(jnp.int32, (1, rows, 1), 1) + r0
        j_idx = lax.broadcasted_iota(jnp.int32, (1, 1, n), 2)
        a_part = a_ref[:, r0:, :]
        d = jnp.sqrt(a_ref[:, k:k + 1, k:k + 1])
        lcol = jnp.where(i_idx >= k, a_part[:, :, k:k + 1] / d, 0.0)
        lrow = jnp.where(j_idx >= k, a_ref[:, k:k + 1, :] / d, 0.0)
        a_ref[:, r0:, :] = a_part - lcol * lrow
        xk = x_ref[:, k:k + 1, :] / d
        b_part = x_ref[:, r0:, :]
        b_part = b_part - jnp.where(i_idx > k, lcol, 0.0) * xk
        x_ref[:, r0:, :] = jnp.where(i_idx == k, xk, b_part)


def chol_solve(square, gram_matrix):
    batch, n, _ = gram_matrix.shape
    spec = pl.BlockSpec((batch, n, n), lambda: (0, 0, 0))
    return pl.pallas_call(
        chol_solve_kernel,
        out_shape=jax.ShapeDtypeStruct(gram_matrix.shape, jnp.float32),
        in_specs=[spec, spec],
        out_specs=spec,
        scratch_shapes=[pltpu.VMEM((batch, n, n), jnp.float32)],
    )(square, gram_matrix)


def mm(spec, a, b):
    return jnp.einsum(spec, a, b, precision=highest)


def solved_rotation(gram_matrix):
    return chol_solve(mm("pij,pjk->pik", gram_matrix, gram_matrix), gram_matrix)


def sum_over_row(x):
    if lax.axis_size("row") != 2:
        return lax.psum(x, "row")
    return x + lax.ppermute(x, "row", [(0, 1), (1, 0)])


def shards(down_proj, act_scale, block_order):
    col_count = lax.axis_size("col")
    me = lax.axis_index("col")
    experts_here, hidden_here, width = down_proj.shape
    block_count = width // BLK
    per_device = block_count // col_count
    panels_here = per_device // 2
    rows_here = experts_here * hidden_here
    columns = jnp.transpose(down_proj, (2, 0, 1)) * act_scale[None, :, :]
    blocks = columns.reshape(block_count, BLK, experts_here, hidden_here)
    span = jnp.arange(per_device + 2, dtype=jnp.int32)

    order = sorted(range(1, col_count), key=lambda d: -min(d, col_count - d)) + [0]
    received = {}
    for d in order:
        dest = (me + d) % col_count
        wanted = (dest * per_device - 2 + span) % block_count
        picked = jnp.take(block_order, wanted, mode="clip")
        piece = jnp.take(blocks, picked, axis=0, mode="clip")
        piece = piece.reshape(panels_here + 1, 2 * BLK, rows_here)
        if d:
            route = [(i, (i + d) % col_count) for i in range(col_count)]
            piece = lax.ppermute(piece, "col", route)
        received[d] = piece
    received = [received[d] for d in range(col_count)]

    grams = sum(mm("pkr,plr->pkl", r, r) for r in received)
    cross = sum(mm("pkr,plr->pkl", r[:-1], r[1:]) for r in received)
    totals = sum_over_row(jnp.concatenate([grams, cross], axis=0))
    grams, cross = totals[: panels_here + 1], totals[panels_here + 1:]

    first = solved_rotation(grams)
    top = first[:-1, :BLK]
    bottom = first[1:, BLK:]
    g_top = mm("pik,pjk->pij", mm("pik,pkl->pil", top, grams[:-1]), top)
    g_bottom = mm("pik,pjk->pij", mm("pik,pkl->pil", bottom, grams[1:]), bottom)
    g_cross = mm("pik,pjk->pij", mm("pik,pkl->pil", top, cross), bottom)
    second_gram = jnp.concatenate(
        [
            jnp.concatenate([g_top, g_cross], axis=2),
            jnp.concatenate([jnp.swapaxes(g_cross, 1, 2), g_bottom], axis=2),
        ],
        axis=1,
    )
    second = solved_rotation(second_gram)
    lead = mm("plk,pkm->plm", second[:, :, :BLK], top)
    trail = mm("plk,pkm->plm", second[:, :, BLK:], bottom)

    out = jnp.zeros((per_device, BLK, experts_here, hidden_here * col_count), jnp.float32)
    for d, r in enumerate(received):
        src = (me - d) % col_count
        part = mm("plk,pkr->plr", lead, r[:-1]) + mm("plk,pkr->plr", trail, r[1:])
        part = part.reshape(per_device, BLK, experts_here, hidden_here)
        out = lax.dynamic_update_slice(out, part, (0, 0, 0, src * hidden_here))
    return out


def solution(mesh):
    return jax.shard_map(
        shards,
        mesh=mesh,
        in_specs=(P(("groups", "row"), "col", None), P(("groups", "row"), "col"), P("groups")),
        out_specs=P(("groups", "col"), None, "row", None),
        check_vma=False,
    )
```

```python
import jax
import jax.numpy as jnp
from jax import lax
from jax.experimental import pallas as pl
from jax.experimental.pallas import tpu as pltpu
from jax.sharding import PartitionSpec as P

BLK = 28


highest = lax.Precision.HIGHEST


def chol_solve_kernel(sq_ref, s_ref, x_ref, a_ref):
    n = sq_ref.shape[1]
    a_ref[...] = sq_ref[...]
    x_ref[...] = s_ref[...]
    for k in range(n):
        r0 = (k // 8) * 8
        rows = n - r0
        i_idx = lax.broadcasted_iota(jnp.int32, (1, rows, 1), 1) + r0
        j_idx = lax.broadcasted_iota(jnp.int32, (1, 1, n), 2)
        a_part = a_ref[:, r0:, :]
        d = jnp.sqrt(a_ref[:, k:k + 1, k:k + 1])
        lcol = jnp.where(i_idx >= k, a_part[:, :, k:k + 1] / d, 0.0)
        lrow = jnp.where(j_idx >= k, a_ref[:, k:k + 1, :] / d, 0.0)
        a_ref[:, r0:, :] = a_part - lcol * lrow
        xk = x_ref[:, k:k + 1, :] / d
        b_part = x_ref[:, r0:, :]
        b_part = b_part - jnp.where(i_idx > k, lcol, 0.0) * xk
        x_ref[:, r0:, :] = jnp.where(i_idx == k, xk, b_part)


def chol_solve(square, gram_matrix):
    batch, n, _ = gram_matrix.shape
    spec = pl.BlockSpec((batch, n, n), lambda: (0, 0, 0))
    return pl.pallas_call(
        chol_solve_kernel,
        out_shape=jax.ShapeDtypeStruct(gram_matrix.shape, jnp.float32),
        in_specs=[spec, spec],
        out_specs=spec,
        scratch_shapes=[pltpu.VMEM((batch, n, n), jnp.float32)],
    )(square, gram_matrix)


def mm(spec, a, b):
    return jnp.einsum(spec, a, b, precision=highest)


def solved_rotation(gram_matrix):
    return chol_solve(mm("pij,pjk->pik", gram_matrix, gram_matrix), gram_matrix)


def sum_over_row(x):
    if lax.axis_size("row") != 2:
        return lax.psum(x, "row")
    return x + lax.ppermute(x, "row", [(0, 1), (1, 0)])


def shards(down_proj, act_scale, block_order):
    col_count = lax.axis_size("col")
    me = lax.axis_index("col")
    experts_here, hidden_here, width = down_proj.shape
    block_count = width // BLK
    per_device = block_count // col_count
    panels_here = per_device // 2
    rows_here = experts_here * hidden_here
    columns = jnp.transpose(down_proj, (2, 0, 1)) * act_scale[None, :, :]
    blocks = columns.reshape(block_count, BLK, experts_here, hidden_here)
    span = jnp.arange(per_device + 2, dtype=jnp.int32)

    order = sorted(range(1, col_count), key=lambda d: -min(d, col_count - d)) + [0]
    received = {}
    for d in order:
        dest = (me + d) % col_count
        wanted = (dest * per_device - 2 + span) % block_count
        picked = jnp.take(block_order, wanted, mode="clip")
        piece = jnp.take(blocks, picked, axis=0, mode="clip")
        piece = piece.reshape(panels_here + 1, 2 * BLK, experts_here, hidden_here)
        if d:
            route = [(i, (i + d) % col_count) for i in range(col_count)]
            piece = lax.ppermute(piece, "col", route)
        received[d] = piece
    received = [received[d] for d in range(col_count)]

    grams = sum(mm("pkeh,pleh->pkl", r, r) for r in received)
    cross = sum(mm("pkeh,pleh->pkl", r[:-1], r[1:]) for r in received)
    totals = sum_over_row(jnp.concatenate([grams, cross], axis=0))
    grams, cross = totals[: panels_here + 1], totals[panels_here + 1:]

    first = solved_rotation(grams)
    top = first[:-1, :BLK]
    bottom = first[1:, BLK:]
    g_top = mm("pik,pjk->pij", mm("pik,pkl->pil", top, grams[:-1]), top)
    g_bottom = mm("pik,pjk->pij", mm("pik,pkl->pil", bottom, grams[1:]), bottom)
    g_cross = mm("pik,pjk->pij", mm("pik,pkl->pil", top, cross), bottom)
    second_gram = jnp.concatenate(
        [
            jnp.concatenate([g_top, g_cross], axis=2),
            jnp.concatenate([jnp.swapaxes(g_cross, 1, 2), g_bottom], axis=2),
        ],
        axis=1,
    )
    second = solved_rotation(second_gram)
    lead = mm("plk,pkm->plm", second[:, :, :BLK], top)
    trail = mm("plk,pkm->plm", second[:, :, BLK:], bottom)

    out = jnp.zeros((per_device, BLK, experts_here, hidden_here * col_count), jnp.float32)
    for d, r in enumerate(received):
        src = (me - d) % col_count
        part = (
            jnp.einsum("plk,pkeh->pleh", lead, r[:-1], precision=lax.Precision.HIGH)
            + jnp.einsum("plk,pkeh->pleh", trail, r[1:], precision=lax.Precision.HIGH)
        )
        part = part.reshape(per_device, BLK, experts_here, hidden_here)
        out = lax.dynamic_update_slice(out, part, (0, 0, 0, src * hidden_here))
    return out


def solution(mesh):
    return jax.shard_map(
        shards,
        mesh=mesh,
        in_specs=(P(("groups", "row"), "col", None), P(("groups", "row"), "col"), P("groups")),
        out_specs=P(("groups", "col"), None, "row", None),
        check_vma=False,
    )
```

```python
import jax
import jax.numpy as jnp
from jax import lax
from jax.experimental import pallas as pl
from jax.experimental.pallas import tpu as pltpu
from jax.sharding import PartitionSpec as P

BLK = 28


highest = lax.Precision.HIGHEST


def chol_solve_kernel(sq_ref, s_ref, x_ref, a_ref):
    n = sq_ref.shape[1]
    a_ref[...] = sq_ref[...]
    x_ref[...] = s_ref[...]
    for k in range(n):
        r0 = (k // 8) * 8
        rows = n - r0
        i_idx = lax.broadcasted_iota(jnp.int32, (1, rows, 1), 1) + r0
        j_idx = lax.broadcasted_iota(jnp.int32, (1, 1, n), 2)
        a_part = a_ref[:, r0:, :]
        d = jnp.sqrt(a_ref[:, k:k + 1, k:k + 1])
        lcol = jnp.where(i_idx >= k, a_part[:, :, k:k + 1] / d, 0.0)
        lrow = jnp.where(j_idx >= k, a_ref[:, k:k + 1, :] / d, 0.0)
        a_ref[:, r0:, :] = a_part - lcol * lrow
        xk = x_ref[:, k:k + 1, :] / d
        b_part = x_ref[:, r0:, :]
        b_part = b_part - jnp.where(i_idx > k, lcol, 0.0) * xk
        x_ref[:, r0:, :] = jnp.where(i_idx == k, xk, b_part)


def chol_solve(square, gram_matrix):
    batch, n, _ = gram_matrix.shape
    spec = pl.BlockSpec((batch, n, n), lambda: (0, 0, 0))
    return pl.pallas_call(
        chol_solve_kernel,
        out_shape=jax.ShapeDtypeStruct(gram_matrix.shape, jnp.float32),
        in_specs=[spec, spec],
        out_specs=spec,
        scratch_shapes=[pltpu.VMEM((batch, n, n), jnp.float32)],
    )(square, gram_matrix)


def mm(spec, a, b):
    return jnp.einsum(spec, a, b, precision=highest)


def solved_rotation(gram_matrix):
    return chol_solve(mm("pij,pjk->pik", gram_matrix, gram_matrix), gram_matrix)


def sum_over_row(x):
    if lax.axis_size("row") != 2:
        return lax.psum(x, "row")
    return x + lax.ppermute(x, "row", [(0, 1), (1, 0)])


def shards(down_proj, act_scale, block_order):
    col_count = lax.axis_size("col")
    me = lax.axis_index("col")
    experts_here, hidden_here, width = down_proj.shape
    block_count = width // BLK
    per_device = block_count // col_count
    panels_here = per_device // 2
    rows_here = experts_here * hidden_here
    columns = jnp.transpose(down_proj, (2, 0, 1))
    scales = lax.all_gather(act_scale, "col")
    blocks = columns.reshape(block_count, BLK, experts_here, hidden_here)
    span = jnp.arange(per_device + 2, dtype=jnp.int32)

    order = sorted(range(1, col_count), key=lambda d: -min(d, col_count - d)) + [0]
    received = {}
    for d in order:
        dest = (me + d) % col_count
        wanted = (dest * per_device - 2 + span) % block_count
        picked = jnp.take(block_order, wanted, mode="clip")
        piece = jnp.take(blocks, picked, axis=0, mode="clip")
        piece = piece.reshape(panels_here + 1, 2 * BLK, experts_here, hidden_here)
        if d:
            route = [(i, (i + d) % col_count) for i in range(col_count)]
            piece = lax.ppermute(piece, "col", route)
        received[d] = piece
    received = [
        received[d] * scales[(me - d) % col_count][None, None, :, :] for d in range(col_count)
    ]

    grams = sum(mm("pkeh,pleh->pkl", r, r) for r in received)
    cross = sum(mm("pkeh,pleh->pkl", r[:-1], r[1:]) for r in received)
    totals = sum_over_row(jnp.concatenate([grams, cross], axis=0))
    grams, cross = totals[: panels_here + 1], totals[panels_here + 1:]

    first = solved_rotation(grams)
    top = first[:-1, :BLK]
    bottom = first[1:, BLK:]
    g_top = mm("pik,pjk->pij", mm("pik,pkl->pil", top, grams[:-1]), top)
    g_bottom = mm("pik,pjk->pij", mm("pik,pkl->pil", bottom, grams[1:]), bottom)
    g_cross = mm("pik,pjk->pij", mm("pik,pkl->pil", top, cross), bottom)
    second_gram = jnp.concatenate(
        [
            jnp.concatenate([g_top, g_cross], axis=2),
            jnp.concatenate([jnp.swapaxes(g_cross, 1, 2), g_bottom], axis=2),
        ],
        axis=1,
    )
    second = solved_rotation(second_gram)
    lead = mm("plk,pkm->plm", second[:, :, :BLK], top)
    trail = mm("plk,pkm->plm", second[:, :, BLK:], bottom)

    out = jnp.zeros((per_device, BLK, experts_here, hidden_here * col_count), jnp.float32)
    for d, r in enumerate(received):
        src = (me - d) % col_count
        part = (
            jnp.einsum("plk,pkeh->pleh", lead, r[:-1], precision=lax.Precision.HIGH)
            + jnp.einsum("plk,pkeh->pleh", trail, r[1:], precision=lax.Precision.HIGH)
        )
        part = part.reshape(per_device, BLK, experts_here, hidden_here)
        out = lax.dynamic_update_slice(out, part, (0, 0, 0, src * hidden_here))
    return out


def solution(mesh):
    return jax.shard_map(
        shards,
        mesh=mesh,
        in_specs=(P(("groups", "row"), "col", None), P(("groups", "row"), "col"), P("groups")),
        out_specs=P(("groups", "col"), None, "row", None),
        check_vma=False,
    )
```

```python
import jax
import jax.numpy as jnp
from jax import lax
from jax.experimental import pallas as pl
from jax.experimental.pallas import tpu as pltpu
from jax.sharding import PartitionSpec as P

BLK = 28


highest = lax.Precision.HIGHEST


def chol_solve_kernel(sq_ref, s_ref, x_ref, a_ref):
    n = sq_ref.shape[1]
    a_ref[...] = sq_ref[...]
    x_ref[...] = s_ref[...]
    for k in range(n):
        r0 = (k // 8) * 8
        rows = n - r0
        i_idx = lax.broadcasted_iota(jnp.int32, (1, rows, 1), 1) + r0
        j_idx = lax.broadcasted_iota(jnp.int32, (1, 1, n), 2)
        a_part = a_ref[:, r0:, :]
        d = jnp.sqrt(a_ref[:, k:k + 1, k:k + 1])
        lcol = jnp.where(i_idx >= k, a_part[:, :, k:k + 1] / d, 0.0)
        lrow = jnp.where(j_idx >= k, a_ref[:, k:k + 1, :] / d, 0.0)
        a_ref[:, r0:, :] = a_part - lcol * lrow
        xk = x_ref[:, k:k + 1, :] / d
        b_part = x_ref[:, r0:, :]
        b_part = b_part - jnp.where(i_idx > k, lcol, 0.0) * xk
        x_ref[:, r0:, :] = jnp.where(i_idx == k, xk, b_part)


def chol_solve(square, gram_matrix):
    batch, n, _ = gram_matrix.shape
    spec = pl.BlockSpec((batch, n, n), lambda: (0, 0, 0))
    return pl.pallas_call(
        chol_solve_kernel,
        out_shape=jax.ShapeDtypeStruct(gram_matrix.shape, jnp.float32),
        in_specs=[spec, spec],
        out_specs=spec,
        scratch_shapes=[pltpu.VMEM((batch, n, n), jnp.float32)],
    )(square, gram_matrix)


def mm(spec, a, b):
    return jnp.einsum(spec, a, b, precision=highest)


def solved_rotation(gram_matrix):
    return chol_solve(mm("pij,pjk->pik", gram_matrix, gram_matrix), gram_matrix)


def sum_over_row(x):
    if lax.axis_size("row") != 2:
        return lax.psum(x, "row")
    return x + lax.ppermute(x, "row", [(0, 1), (1, 0)])


def shards(down_proj, act_scale, block_order):
    col_count = lax.axis_size("col")
    me = lax.axis_index("col")
    experts_here, hidden_here, width = down_proj.shape
    block_count = width // BLK
    per_device = block_count // col_count
    panels_here = per_device // 2
    rows_here = experts_here * hidden_here
    columns = jnp.transpose(down_proj, (2, 0, 1))
    scales = lax.all_gather(act_scale, "col")
    columns, scales = lax.optimization_barrier((columns, scales))
    blocks = columns.reshape(block_count, BLK, experts_here, hidden_here)
    span = jnp.arange(per_device + 2, dtype=jnp.int32)

    order = sorted(range(1, col_count), key=lambda d: -min(d, col_count - d)) + [0]
    received = {}
    for d in order:
        dest = (me + d) % col_count
        wanted = (dest * per_device - 2 + span) % block_count
        picked = jnp.take(block_order, wanted, mode="clip")
        piece = jnp.take(blocks, picked, axis=0, mode="clip")
        piece = piece.reshape(panels_here + 1, 2 * BLK, experts_here, hidden_here)
        if d:
            route = [(i, (i + d) % col_count) for i in range(col_count)]
            piece = lax.ppermute(piece, "col", route)
        received[d] = piece
    received = [
        received[d] * scales[(me - d) % col_count][None, None, :, :] for d in range(col_count)
    ]

    grams = sum(mm("pkeh,pleh->pkl", r, r) for r in received)
    cross = sum(mm("pkeh,pleh->pkl", r[:-1], r[1:]) for r in received)
    totals = sum_over_row(jnp.concatenate([grams, cross], axis=0))
    grams, cross = totals[: panels_here + 1], totals[panels_here + 1:]

    first = solved_rotation(grams)
    top = first[:-1, :BLK]
    bottom = first[1:, BLK:]
    g_top = mm("pik,pjk->pij", mm("pik,pkl->pil", top, grams[:-1]), top)
    g_bottom = mm("pik,pjk->pij", mm("pik,pkl->pil", bottom, grams[1:]), bottom)
    g_cross = mm("pik,pjk->pij", mm("pik,pkl->pil", top, cross), bottom)
    second_gram = jnp.concatenate(
        [
            jnp.concatenate([g_top, g_cross], axis=2),
            jnp.concatenate([jnp.swapaxes(g_cross, 1, 2), g_bottom], axis=2),
        ],
        axis=1,
    )
    second = solved_rotation(second_gram)
    lead = mm("plk,pkm->plm", second[:, :, :BLK], top)
    trail = mm("plk,pkm->plm", second[:, :, BLK:], bottom)

    out = jnp.zeros((per_device, BLK, experts_here, hidden_here * col_count), jnp.float32)
    for d, r in enumerate(received):
        src = (me - d) % col_count
        part = (
            jnp.einsum("plk,pkeh->pleh", lead, r[:-1], precision=lax.Precision.HIGH)
            + jnp.einsum("plk,pkeh->pleh", trail, r[1:], precision=lax.Precision.HIGH)
        )
        part = part.reshape(per_device, BLK, experts_here, hidden_here)
        out = lax.dynamic_update_slice(out, part, (0, 0, 0, src * hidden_here))
    return out


def solution(mesh):
    return jax.shard_map(
        shards,
        mesh=mesh,
        in_specs=(P(("groups", "row"), "col", None), P(("groups", "row"), "col"), P("groups")),
        out_specs=P(("groups", "col"), None, "row", None),
        check_vma=False,
    )
```
